256 devices in a mesh: chan: 32 (over y_hi, z, core), win: 8 (over x, y_lo).
Axes of the slice: x: 4, y: 4 (y_hi: 2, y_lo: 2; y = y_hi * 2 + y_lo), z: 8, core: 2. Of those that a mesh axis runs over, the one named last changes fastest.
Arguments:
- traces: bfloat16 [8, 1024, 8192], P('win', 'chan'), may hold values from -6 to 6
- owner: int32 [3], replicated, may hold values from 0 to 31
- window_mask: int32 [8, 32], P('win', 'chan'), may hold values 0 or 1
Outputs:
- stacks: float32 [3, 32, 64, 1024], P(None, None, 'win', 'chan')
The draws below stay inside these ranges and needn't reach their ends.
Inputs may be any that keep to these rules, and one draw needn't show every extreme that they name: `owner`: each step names one channel block.
All inputs are finite; a program needn't handle non-finite values. No bound on the sum of `window_mask` on one device may be relied on, other than what follows from the above.
Results may differ from the reference program's by a relative error of at most 0.0028.
Values may be sent and summed in bfloat16 or wider, within the bound.
No kernel may reach another device: no remote copies, remote signals or barrier semaphores. Data moves between devices by JAX's collectives and lax.ppermute only.
A program may use at most 128 MiB of HBM per device.

```python
import jax
import jax.numpy as jnp
from jax import lax

S = 8192
LAGS = 64
STEPS = 3
CHANNELS = 1024
WINDOWS = 8
N_CHAN = 32


def with_ends(entries, key, least, high):
    extent = entries.shape
    place = [jax.random.randint(jax.random.fold_in(key, axis), (), 0, extent[axis]) for axis in range(len(extent))]
    entries = entries.at[tuple(place)].set(least)
    longest = extent.index(max(extent))
    place[longest] = (place[longest] + 1) % extent[longest]
    return entries.at[tuple(place)].set(high)


def shard_levels(stream_key, extent, cuts, low, high):
    level, own = 1.0, jax.random.fold_in(stream_key, 6)
    for position, blocks in cuts:
        heights = jnp.exp(jax.random.uniform(jax.random.fold_in(own, position), (blocks,), jnp.float32, low / len(cuts), high / len(cuts)))
        level = level * jnp.repeat(heights, extent[position] // blocks).reshape([-1 if axis == position else 1 for axis in range(len(extent))])
    return level


def scatter_about(stream_key, shape, spread, limit, pieces=(), kind=jnp.bfloat16):
    result = spread * jax.random.normal(stream_key, shape, jnp.float32)
    if pieces:
        result = result * shard_levels(stream_key, shape, pieces, -0.22, 0.18)
    return jnp.clip(result, -limit, limit).astype(kind)


def setup_inputs(seed: int = 0) -> dict:
    keys = jax.random.split(jax.random.key(seed), 4)
    return {
        "traces": scatter_about(keys[0], (WINDOWS, CHANNELS, S), 1.0, 6.0, ((0, 8), (1, 32))),
        "owner": jax.random.randint(keys[1], (STEPS,), 0, N_CHAN).astype(jnp.int32),
        "window_mask": with_ends((jax.random.randint(keys[2], (WINDOWS, N_CHAN), 0, 4) < 3).astype(jnp.int32), jax.random.fold_in(keys[2], 1), 0, 1),
    }


def reference(traces, owner, window_mask):
    signal = traces.astype(jnp.float32)
    whitened = (signal * lax.rsqrt(lax.optimization_barrier(jnp.mean(signal * signal, axis=-1, keepdims=True)) + 1e-06)).astype(jnp.bfloat16)
    windows, channels, samples = traces.shape
    chan_dev = channels // N_CHAN
    flags = window_mask.astype(jnp.float32)
    column_flags = jnp.repeat(flags, chan_dev, axis=1)
    padded = jnp.pad(whitened, ((0, 0), (0, 0), (LAGS // 2, LAGS // 2)))
    factor = 1.0 / jnp.sqrt(jnp.float32(samples))
    outputs = []
    for step in range(STEPS):
        block_index = owner[step].astype(jnp.int32)
        source = lax.dynamic_slice_in_dim(whitened, block_index * chan_dev, chan_dev, 1)
        source_flag = lax.dynamic_slice_in_dim(flags, block_index, 1, 1)
        source = source * source_flag[:, :, None].astype(jnp.bfloat16)

        def one_lag(lag_index):
            shifted = lax.dynamic_slice_in_dim(padded, lag_index, samples, 2)
            summed = jnp.zeros((chan_dev, channels), jnp.float32)
            for window in range(windows):
                product = jnp.dot(source[window], shifted[window].T, preferred_element_type=jnp.float32)
                summed = summed + product * column_flags[window][None, :] * factor
            return summed
        lagged = lax.map(one_lag, jnp.arange(LAGS, dtype=jnp.int32))
        outputs.append(jnp.transpose(lagged, (1, 0, 2)))
    return jnp.stack(outputs)
```

```python
import math

import jax
import jax.numpy as jnp
from jax import lax
from jax.sharding import PartitionSpec as P

LAGS = 64
CHAN_BITS = (0, 1, 4, 2, 3)
WIN_BITS = (0, 1, 2)


def xor_pairs(size, bit):
    return [(i, i ^ (1 << bit)) for i in range(size)]


def broadcast(value, me, owner_index, axis, size):
    masked = jnp.where(me == owner_index, value, jnp.zeros_like(value))
    rows, samples = masked.shape
    pieces = masked.reshape(rows, size, samples // size)
    for bit in CHAN_BITS:
        half = pieces.shape[1] // 2
        low, high = pieces[:, :half], pieces[:, half:]
        mine = ((me >> bit) & 1) == 0
        send = jnp.where(mine, high, low)
        keep = jnp.where(mine, low, high)
        pieces = keep + lax.ppermute(send, axis, xor_pairs(size, bit))
    for bit in reversed(CHAN_BITS):
        mine = ((me >> bit) & 1) == 0
        got = lax.ppermute(pieces, axis, xor_pairs(size, bit))
        pieces = jnp.where(
            mine, jnp.concatenate([pieces, got], 1), jnp.concatenate([got, pieces], 1)
        )
    return pieces.reshape(rows, samples)


def scatter_lags(complete, me, axis, size):
    rows, lags, chan = complete.shape
    bits = size.bit_length() - 1
    parts = complete.reshape(rows, *([2] * bits), lags // size, chan)
    remaining = list(reversed(range(bits)))
    for bit in WIN_BITS:
        where = 1 + remaining.index(bit)
        remaining.remove(bit)
        mine = ((me >> bit) & 1) == 0
        low = lax.index_in_dim(parts, 0, where, keepdims=False)
        high = lax.index_in_dim(parts, 1, where, keepdims=False)
        send = jnp.where(mine, high, low)
        keep = jnp.where(mine, low, high)
        parts = keep + lax.ppermute(send, axis, xor_pairs(size, bit))
    return parts


def body(traces, owner, window_mask):
    chan_dev = traces.shape[1]
    samples = traces.shape[2]
    step_count = owner.shape[0]
    chan_size = lax.axis_size("chan")
    win_size = lax.axis_size("win")
    chan_me = lax.axis_index("chan")
    win_me = lax.axis_index("win")
    signal = traces[0].astype(jnp.float32)
    whitened = (
        signal * lax.rsqrt(jnp.mean(signal * signal, axis=-1, keepdims=True) + 1e-06)
    ).astype(jnp.bfloat16)
    own_flag = window_mask[0, 0].astype(jnp.float32)
    outgoing = whitened * own_flag.astype(jnp.bfloat16)
    padded = jnp.pad(whitened, ((0, 0), (64, 64)))
    half_lags = LAGS // 2
    per_dev = LAGS // win_size
    time_block = min(samples, 4096)
    factor = own_flag / math.sqrt(samples)

    def correlate(sources, lag_values):
        summed = jnp.zeros((sources.shape[0], len(lag_values), chan_dev), jnp.float32)
        for offset in range(0, samples, time_block):
            shifted = jnp.stack(
                [
                    padded[
                        :,
                        offset + lag - half_lags + 64 : offset + lag - half_lags + 64 + time_block,
                    ]
                    for lag in lag_values
                ],
                0,
            )
            summed = summed + jnp.einsum(
                "pt,gct->pgc",
                sources[:, offset : offset + time_block],
                shifted,
                preferred_element_type=jnp.float32,
            )
        return summed * factor

    results = []
    for step in range(step_count):
        source = broadcast(outgoing, chan_me, owner[step], "chan", chan_size)
        complete = jnp.concatenate(
            [correlate(source, list(range(g * 8, g * 8 + 8))) for g in range(LAGS // 8)], 1
        )
        results.append(complete)
    complete = jnp.concatenate(results, 0)
    reduced = scatter_lags(complete, win_me, "win", win_size)
    return reduced.reshape(step_count, chan_dev, per_dev, chan_dev)


def solution(mesh):
    return jax.shard_map(
        body,
        mesh=mesh,
        in_specs=(P("win", "chan", None), P(), P("win", "chan")),
        out_specs=P(None, None, "win", "chan"),
        check_vma=False,
    )
```

```python
import math

import jax
import jax.numpy as jnp
from jax import lax
from jax.experimental import pallas as pl
from jax.experimental.pallas import tpu as pltpu
from jax.sharding import PartitionSpec as P

LAGS = 64
EDGE = 64
TIME_BLOCK = 1024
CHAN_BITS = (0, 1, 4, 2, 3)
WIN_BITS = (0, 1, 2)


def xor_pairs(size, bit):
    return [(i, i ^ (1 << bit)) for i in range(size)]


def broadcast(masked, me, axis, size):
    rows, samples = masked.shape
    pieces = masked.reshape(rows, size, samples // size)
    for bit in CHAN_BITS:
        half = pieces.shape[1] // 2
        low, high = pieces[:, :half], pieces[:, half:]
        mine = ((me >> bit) & 1) == 0
        send = jnp.where(mine, high, low)
        keep = jnp.where(mine, low, high)
        pieces = keep + lax.ppermute(send, axis, xor_pairs(size, bit))
    for bit in reversed(CHAN_BITS):
        mine = ((me >> bit) & 1) == 0
        got = lax.ppermute(pieces, axis, xor_pairs(size, bit))
        pieces = jnp.where(
            mine, jnp.concatenate([pieces, got], 1), jnp.concatenate([got, pieces], 1)
        )
    return pieces.reshape(rows, samples)


def scatter_lags(complete, me, axis, size):
    lags = complete.shape[0]
    bits = size.bit_length() - 1
    parts = complete.reshape(*([2] * bits), lags // size, *complete.shape[1:])
    remaining = list(reversed(range(bits)))
    for bit in WIN_BITS:
        where = remaining.index(bit)
        remaining.remove(bit)
        mine = ((me >> bit) & 1) == 0
        low = lax.index_in_dim(parts, 0, where, keepdims=False)
        high = lax.index_in_dim(parts, 1, where, keepdims=False)
        send = jnp.where(mine, high, low)
        keep = jnp.where(mine, low, high)
        parts = keep + lax.ppermute(send, axis, xor_pairs(size, bit))
    return parts


def correlate(sources, padded, chan_dev):
    rows, samples = sources.shape
    width = TIME_BLOCK + 128

    def kernel(src_ref, w_ref, out_ref):
        def block(k, acc):
            base = pl.multiple_of(k * TIME_BLOCK, TIME_BLOCK)
            window = w_ref[:, pl.ds(base, width)]
            parts = [
                pltpu.roll(window, width - (EDGE - LAGS // 2 + lag), 1)[:, :TIME_BLOCK]
                for lag in range(LAGS)
            ]
            stacked = jnp.concatenate(parts, 0)
            chunk = src_ref[:, pl.ds(base, TIME_BLOCK)]
            return acc + lax.dot_general(
                stacked, chunk, (((1,), (1,)), ((), ())), preferred_element_type=jnp.float32
            )

        out_ref[...] = lax.fori_loop(
            0, samples // TIME_BLOCK, block, jnp.zeros((LAGS * chan_dev, rows), jnp.float32)
        )

    return pl.pallas_call(
        kernel,
        out_shape=jax.ShapeDtypeStruct((LAGS * chan_dev, rows), jnp.float32),
        in_specs=[
            pl.BlockSpec(memory_space=pltpu.VMEM),
            pl.BlockSpec(memory_space=pltpu.VMEM),
        ],
        out_specs=pl.BlockSpec(memory_space=pltpu.VMEM),
    )(sources, padded)


def body(traces, owner, window_mask):
    chan_dev = traces.shape[1]
    samples = traces.shape[2]
    step_count = owner.shape[0]
    chan_size = lax.axis_size("chan")
    win_size = lax.axis_size("win")
    chan_me = lax.axis_index("chan")
    win_me = lax.axis_index("win")
    signal = traces[0].astype(jnp.float32)
    whitened = (
        signal * lax.rsqrt(jnp.mean(signal * signal, axis=-1, keepdims=True) + 1e-06)
    ).astype(jnp.bfloat16)
    own_flag = window_mask[0, 0].astype(jnp.float32)
    outgoing = whitened * own_flag.astype(jnp.bfloat16)
    masked = jnp.concatenate(
        [jnp.where(chan_me == owner[step], outgoing, jnp.zeros_like(outgoing)) for step in range(step_count)],
        0,
    )
    sources = broadcast(masked, chan_me, "chan", chan_size)
    padded = jnp.pad(whitened, ((0, 0), (EDGE, EDGE)))
    factor = own_flag / math.sqrt(samples)
    complete = correlate(sources, padded, chan_dev) * factor
    complete = complete.reshape(LAGS, chan_dev, step_count * chan_dev)
    reduced = scatter_lags(complete, win_me, "win", win_size)
    per_dev = LAGS // win_size
    reduced = reduced.reshape(per_dev, chan_dev, step_count, chan_dev)
    return jnp.transpose(reduced, (2, 3, 0, 1))


def solution(mesh):
    return jax.shard_map(
        body,
        mesh=mesh,
        in_specs=(P("win", "chan", None), P(), P("win", "chan")),
        out_specs=P(None, None, "win", "chan"),
        check_vma=False,
    )
```

```python
import math

import jax
import jax.numpy as jnp
from jax import lax
from jax.experimental import pallas as pl
from jax.experimental.pallas import tpu as pltpu
from jax.sharding import PartitionSpec as P

LAGS = 64
EDGE = 64
TIME_BLOCK = 1024
CHAN_BITS = ((0, 1, 4, 2, 3), (0, 4, 1, 2, 3))
WIN_BITS = ((0, 1, 2), (1, 0, 2))


def xor_pairs(size, bit):
    return [(i, i ^ (1 << bit)) for i in range(size)]


def broadcast(masked, me, axis, size, order):
    rows, samples = masked.shape
    pieces = masked.reshape(rows, size, samples // size)
    for bit in order:
        half = pieces.shape[1] // 2
        low, high = pieces[:, :half], pieces[:, half:]
        mine = ((me >> bit) & 1) == 0
        send = jnp.where(mine, high, low)
        keep = jnp.where(mine, low, high)
        pieces = keep + lax.ppermute(send, axis, xor_pairs(size, bit))
    for bit in reversed(order):
        mine = ((me >> bit) & 1) == 0
        got = lax.ppermute(pieces, axis, xor_pairs(size, bit))
        pieces = jnp.where(
            mine, jnp.concatenate([pieces, got], 1), jnp.concatenate([got, pieces], 1)
        )
    return pieces.reshape(rows, samples)


def scatter_lags(complete, me, axis, size, order):
    lags = complete.shape[0]
    bits = size.bit_length() - 1
    parts = complete.reshape(*([2] * bits), lags // size, *complete.shape[1:])
    remaining = list(reversed(range(bits)))
    for bit in order:
        where = remaining.index(bit)
        remaining.remove(bit)
        mine = ((me >> bit) & 1) == 0
        low = lax.index_in_dim(parts, 0, where, keepdims=False)
        high = lax.index_in_dim(parts, 1, where, keepdims=False)
        send = jnp.where(mine, high, low)
        keep = jnp.where(mine, low, high)
        parts = keep + lax.ppermute(send, axis, xor_pairs(size, bit))
    return parts


def correlate(sources, padded, chan_dev):
    rows, samples = sources.shape
    width = TIME_BLOCK + 128

    def kernel(src_ref, w_ref, out_ref):
        def block(k, acc):
            base = pl.multiple_of(k * TIME_BLOCK, TIME_BLOCK)
            window = w_ref[:, pl.ds(base, width)]
            parts = [
                pltpu.roll(window, width - (EDGE - LAGS // 2 + lag), 1)[:, :TIME_BLOCK]
                for lag in range(LAGS)
            ]
            stacked = jnp.concatenate(parts, 0)
            chunk = src_ref[:, pl.ds(base, TIME_BLOCK)]
            return acc + lax.dot_general(
                stacked, chunk, (((1,), (1,)), ((), ())), preferred_element_type=jnp.float32
            )

        out_ref[...] = lax.fori_loop(
            0, samples // TIME_BLOCK, block, jnp.zeros((LAGS * chan_dev, rows), jnp.float32)
        )

    return pl.pallas_call(
        kernel,
        out_shape=jax.ShapeDtypeStruct((LAGS * chan_dev, rows), jnp.float32),
        in_specs=[
            pl.BlockSpec(memory_space=pltpu.VMEM),
            pl.BlockSpec(memory_space=pltpu.VMEM),
        ],
        out_specs=pl.BlockSpec(memory_space=pltpu.VMEM),
    )(sources, padded)


def body(traces, owner, window_mask):
    chan_dev = traces.shape[1]
    samples = traces.shape[2]
    step_count = owner.shape[0]
    chan_size = lax.axis_size("chan")
    win_size = lax.axis_size("win")
    chan_me = lax.axis_index("chan")
    win_me = lax.axis_index("win")
    signal = traces[0].astype(jnp.float32)
    whitened = (
        signal * lax.rsqrt(jnp.mean(signal * signal, axis=-1, keepdims=True) + 1e-06)
    ).astype(jnp.bfloat16)
    own_flag = window_mask[0, 0].astype(jnp.float32)
    outgoing = whitened * own_flag.astype(jnp.bfloat16)
    masked = jnp.concatenate(
        [jnp.where(chan_me == owner[step], outgoing, jnp.zeros_like(outgoing)) for step in range(step_count)],
        0,
    )
    rows = masked.shape[0] // 2
    sources = jnp.concatenate(
        [
            broadcast(masked[which * rows : (which + 1) * rows], chan_me, "chan", chan_size, order)
            for which, order in enumerate(CHAN_BITS)
        ],
        0,
    )
    padded = jnp.pad(whitened, ((0, 0), (EDGE, EDGE)))
    factor = own_flag / math.sqrt(samples)
    complete = correlate(sources, padded, chan_dev) * factor
    complete = complete.reshape(LAGS, chan_dev, step_count * chan_dev)
    cols = complete.shape[-1] // 2
    reduced = jnp.concatenate(
        [
            scatter_lags(complete[..., which * cols : (which + 1) * cols], win_me, "win", win_size, order)
            for which, order in enumerate(WIN_BITS)
        ],
        -1,
    )
    per_dev = LAGS // win_size
    reduced = reduced.reshape(per_dev, chan_dev, step_count, chan_dev)
    return jnp.transpose(reduced, (2, 3, 0, 1))


def solution(mesh):
    return jax.shard_map(
        body,
        mesh=mesh,
        in_specs=(P("win", "chan", None), P(), P("win", "chan")),
        out_specs=P(None, None, "win", "chan"),
        check_vma=False,
    )
```

```python
import math

import jax
import jax.numpy as jnp
from jax import lax
from jax.experimental import pallas as pl
from jax.experimental.pallas import tpu as pltpu
from jax.sharding import PartitionSpec as P

LAGS = 64
EDGE = 64
TIME_BLOCK = 2048
CHAN_BITS = ((0, 1, 4, 2, 3), (0, 4, 1, 2, 3))
WIN_BITS = ((0, 1, 2), (1, 0, 2))


def xor_pairs(size, bit):
    return [(i, i ^ (1 << bit)) for i in range(size)]


def broadcast(masked, me, axis, size, order):
    pieces = masked
    for bit in order:
        half = pieces.shape[0] // 2
        low, high = pieces[:half], pieces[half:]
        mine = ((me >> bit) & 1) == 0
        send = jnp.where(mine, high, low)
        keep = jnp.where(mine, low, high)
        pieces = keep + lax.ppermute(send, axis, xor_pairs(size, bit))
    for bit in reversed(order):
        mine = ((me >> bit) & 1) == 0
        got = lax.ppermute(pieces, axis, xor_pairs(size, bit))
        pieces = jnp.where(
            mine, jnp.concatenate([pieces, got], 0), jnp.concatenate([got, pieces], 0)
        )
    return pieces


def scatter_lags(complete, me, axis, size, order):
    rows, width = complete.shape
    bits = size.bit_length() - 1
    parts = complete.reshape(rows, *([2] * bits), width // size)
    remaining = list(reversed(range(bits)))
    for bit in order:
        where = 1 + remaining.index(bit)
        remaining.remove(bit)
        mine = ((me >> bit) & 1) == 0
        low = lax.index_in_dim(parts, 0, where, keepdims=False)
        high = lax.index_in_dim(parts, 1, where, keepdims=False)
        send = jnp.where(mine, high, low)
        keep = jnp.where(mine, low, high)
        parts = keep + lax.ppermute(send, axis, xor_pairs(size, bit))
    return parts


def correlate(sources, padded, chan_dev):
    piece_count, rows, piece_width = sources.shape
    samples = piece_count * piece_width
    per_block = TIME_BLOCK // piece_width
    width = TIME_BLOCK + 128

    def kernel(src_ref, w_ref, out_ref):
        def block(k, acc):
            base = pl.multiple_of(k * TIME_BLOCK, TIME_BLOCK)
            window = w_ref[:, pl.ds(base, width)]
            parts = [
                pltpu.roll(window, width - (EDGE - LAGS // 2 + lag), 1)[:, :TIME_BLOCK]
                for lag in range(LAGS)
            ]
            stacked = jnp.concatenate(parts, 0)
            first = pl.multiple_of(k * per_block, per_block)
            chunk = jnp.concatenate([src_ref[first + j] for j in range(per_block)], 1)
            return acc + lax.dot_general(
                stacked, chunk, (((1,), (1,)), ((), ())), preferred_element_type=jnp.float32
            )

        out_ref[...] = lax.fori_loop(
            0, samples // TIME_BLOCK, block, jnp.zeros((LAGS * chan_dev, rows), jnp.float32)
        ).T

    return pl.pallas_call(
        kernel,
        out_shape=jax.ShapeDtypeStruct((rows, LAGS * chan_dev), jnp.float32),
        in_specs=[
            pl.BlockSpec(memory_space=pltpu.VMEM),
            pl.BlockSpec(memory_space=pltpu.VMEM),
        ],
        out_specs=pl.BlockSpec(memory_space=pltpu.VMEM),
    )(sources, padded)


def body(traces, owner, window_mask):
    chan_dev = traces.shape[1]
    samples = traces.shape[2]
    step_count = owner.shape[0]
    chan_size = lax.axis_size("chan")
    win_size = lax.axis_size("win")
    chan_me = lax.axis_index("chan")
    win_me = lax.axis_index("win")
    signal = traces[0].astype(jnp.float32)
    whitened = (
        signal * lax.rsqrt(jnp.mean(signal * signal, axis=-1, keepdims=True) + 1e-06)
    ).astype(jnp.bfloat16)
    own_flag = window_mask[0, 0].astype(jnp.float32)
    outgoing = whitened * own_flag.astype(jnp.bfloat16)
    masked = jnp.concatenate(
        [jnp.where(chan_me == owner[step], outgoing, jnp.zeros_like(outgoing)) for step in range(step_count)],
        0,
    )
    rows = masked.shape[0]
    masked = masked.reshape(rows, chan_size, samples // chan_size).transpose(1, 0, 2)
    half = rows // 2
    sources = jnp.concatenate(
        [
            broadcast(masked[:, which * half : (which + 1) * half], chan_me, "chan", chan_size, order)
            for which, order in enumerate(CHAN_BITS)
        ],
        1,
    )
    padded = jnp.pad(whitened, ((0, 0), (EDGE, EDGE)))
    factor = own_flag / math.sqrt(samples)
    complete = correlate(sources, padded, chan_dev) * factor
    reduced = jnp.concatenate(
        [
            scatter_lags(complete[which * half : (which + 1) * half], win_me, "win", win_size, order)
            for which, order in enumerate(WIN_BITS)
        ],
        0,
    )
    per_dev = LAGS // win_size
    return reduced.reshape(step_count, chan_dev, per_dev, chan_dev)


def solution(mesh):
    return jax.shard_map(
        body,
        mesh=mesh,
        in_specs=(P("win", "chan", None), P(), P("win", "chan")),
        out_specs=P(None, None, "win", "chan"),
        check_vma=False,
    )
```

```python
import math

import jax
import jax.numpy as jnp
from jax import lax
from jax.experimental import pallas as pl
from jax.experimental.pallas import tpu as pltpu
from jax.sharding import PartitionSpec as P

LAGS = 64
EDGE = 128
TIME_BLOCK = 2048
CHAN_BITS = ((0, 1, 4, 2, 3), (0, 4, 1, 2, 3))

def xor_pairs(size, bit):
    return [(i, i ^ (1 << bit)) for i in range(size)]


def broadcast(masked, me, axis, size, order):
    pieces = masked
    for bit in order:
        half = pieces.shape[0] // 2
        low, high = pieces[:half], pieces[half:]
        mine = ((me >> bit) & 1) == 0
        send = jnp.where(mine, high, low)
        keep = jnp.where(mine, low, high)
        pieces = keep + lax.ppermute(send, axis, xor_pairs(size, bit))
    for bit in reversed(order):
        mine = ((me >> bit) & 1) == 0
        got = lax.ppermute(pieces, axis, xor_pairs(size, bit))
        pieces = jnp.where(
            mine, jnp.concatenate([pieces, got], 0), jnp.concatenate([got, pieces], 0)
        )
    return pieces


def correlate(halves, whitened, factor, blocks):
    piece_count, rows_half, piece_width = halves[0].shape
    rows = rows_half * len(halves)
    chan_dev, samples = whitened.shape
    per_block = TIME_BLOCK // piece_width
    width = TIME_BLOCK + 2 * EDGE
    out_width = LAGS * chan_dev // blocks

    def kernel(factor_ref, *refs):
        src_refs, w_ref, out_ref, pad_ref = refs[: len(halves)], refs[len(halves)], refs[-2], refs[-1]
        pad_ref[:, :EDGE] = jnp.zeros((chan_dev, EDGE), pad_ref.dtype)
        pad_ref[:, EDGE + samples :] = jnp.zeros((chan_dev, EDGE), pad_ref.dtype)
        pad_ref[:, EDGE : EDGE + samples] = w_ref[...]

        def block(k, acc):
            base = pl.multiple_of(k * TIME_BLOCK, TIME_BLOCK)
            window = pad_ref[:, pl.ds(base, width)]
            parts = [
                pltpu.roll(window, width - (EDGE - LAGS // 2 + lag), 1)[:, :TIME_BLOCK]
                for lag in range(LAGS)
            ]
            stacked = jnp.concatenate(parts, 0)
            first = pl.multiple_of(k * per_block, per_block)
            chunk = jnp.concatenate(
                [
                    jnp.concatenate([src_ref[first + j] for j in range(per_block)], 1)
                    for src_ref in src_refs
                ],
                0,
            )
            return acc + lax.dot_general(
                stacked, chunk, (((1,), (1,)), ((), ())), preferred_element_type=jnp.float32
            )

        acc = lax.fori_loop(
            0, samples // TIME_BLOCK, block, jnp.zeros((LAGS * chan_dev, rows), jnp.float32)
        )
        result = acc.T * factor_ref[0, 0]
        for j in range(blocks):
            out_ref[j] = result[:, j * out_width : (j + 1) * out_width]

    return pl.pallas_call(
        kernel,
        out_shape=jax.ShapeDtypeStruct((blocks, rows, out_width), jnp.float32),
        in_specs=[pl.BlockSpec(memory_space=pltpu.SMEM)]
        + [pl.BlockSpec(memory_space=pltpu.VMEM) for _ in range(len(halves) + 1)],
        out_specs=pl.BlockSpec(memory_space=pltpu.VMEM),
        scratch_shapes=[pltpu.VMEM((chan_dev, samples + 2 * EDGE), whitened.dtype)],
    )(factor.reshape(1, 1), *halves, whitened)


def body(traces, owner, window_mask):
    chan_dev = traces.shape[1]
    samples = traces.shape[2]
    step_count = owner.shape[0]
    chan_size = lax.axis_size("chan")
    win_size = lax.axis_size("win")
    chan_me = lax.axis_index("chan")
    win_me = lax.axis_index("win")
    signal = traces[0].astype(jnp.float32)
    whitened = (
        signal * lax.rsqrt(jnp.mean(signal * signal, axis=-1, keepdims=True) + 1e-06)
    ).astype(jnp.bfloat16)
    own_flag = window_mask[0, 0].astype(jnp.float32)
    outgoing = whitened * own_flag.astype(jnp.bfloat16)
    masked = jnp.concatenate(
        [jnp.where(chan_me == owner[step], outgoing, jnp.zeros_like(outgoing)) for step in range(step_count)],
        0,
    )
    rows = masked.shape[0]
    masked = masked.reshape(rows, chan_size, samples // chan_size).transpose(1, 0, 2)
    half = rows // 2
    halves = [
        broadcast(masked[:, which * half : (which + 1) * half], chan_me, "chan", chan_size, order)
        for which, order in enumerate(CHAN_BITS)
    ]
    factor = own_flag / math.sqrt(samples)
    complete = correlate(halves, whitened, factor, win_size)
    reduced = jnp.sum(lax.all_to_all(complete, "win", 0, 0, tiled=True), 0)
    per_dev = LAGS // win_size
    return reduced.reshape(step_count, chan_dev, per_dev, chan_dev)


def solution(mesh):
    return jax.shard_map(
        body,
        mesh=mesh,
        in_specs=(P("win", "chan", None), P(), P("win", "chan")),
        out_specs=P(None, None, "win", "chan"),
        check_vma=False,
    )
```

```python
import math

import jax
import jax.numpy as jnp
from jax import lax
from jax.experimental import pallas as pl
from jax.experimental.pallas import tpu as pltpu
from jax.sharding import PartitionSpec as P

LAGS = 64
EDGE = 128
TIME_BLOCK = 2048
CHAN_BITS = (((0,), (1,), (4,), (2, 3)), ((0,), (4,), (1,), (2, 3)))

def digit_of(me, bits):
    digit = 0
    for bit in bits:
        digit = digit * 2 + ((me >> bit) & 1)
    return digit


def flip_mask(bits, offset):
    mask = 0
    for place, bit in enumerate(bits):
        if (offset >> (len(bits) - 1 - place)) & 1:
            mask |= 1 << bit
    return mask


def xor_pairs(size, mask):
    return [(i, i ^ mask) for i in range(size)]


def broadcast(masked, me, axis, size, order):
    pieces = masked
    for bits in order:
        radix = 1 << len(bits)
        quarters = pieces.reshape(radix, pieces.shape[0] // radix, *pieces.shape[1:])
        digit = digit_of(me, bits)
        pieces = lax.dynamic_index_in_dim(quarters, digit, 0, keepdims=False)
        for offset in range(1, radix):
            send = lax.dynamic_index_in_dim(quarters, digit ^ offset, 0, keepdims=False)
            pieces = pieces + lax.ppermute(send, axis, xor_pairs(size, flip_mask(bits, offset)))
    for bits in reversed(order):
        radix = 1 << len(bits)
        digit = digit_of(me, bits)
        got = [pieces] + [
            lax.ppermute(pieces, axis, xor_pairs(size, flip_mask(bits, offset)))
            for offset in range(1, radix)
        ]
        slots = []
        for slot in range(radix):
            offset = slot ^ digit
            value = got[0]
            for other in range(1, radix):
                value = jnp.where(offset == other, got[other], value)
            slots.append(value)
        pieces = jnp.concatenate(slots, 0)
    return pieces


def correlate(halves, whitened, factor, blocks):
    piece_count, rows_half, piece_width = halves[0].shape
    rows = rows_half * len(halves)
    chan_dev, samples = whitened.shape
    per_block = TIME_BLOCK // piece_width
    width = TIME_BLOCK + 2 * EDGE
    out_width = LAGS * chan_dev // blocks

    def kernel(factor_ref, *refs):
        src_refs, w_ref, out_ref, pad_ref = refs[: len(halves)], refs[len(halves)], refs[-2], refs[-1]
        pad_ref[:, :EDGE] = jnp.zeros((chan_dev, EDGE), pad_ref.dtype)
        pad_ref[:, EDGE + samples :] = jnp.zeros((chan_dev, EDGE), pad_ref.dtype)
        pad_ref[:, EDGE : EDGE + samples] = w_ref[...]

        def block(k, acc):
            base = pl.multiple_of(k * TIME_BLOCK, TIME_BLOCK)
            window = pad_ref[:, pl.ds(base, width)]
            parts = [
                pltpu.roll(window, width - (EDGE - LAGS // 2 + lag), 1)[:, :TIME_BLOCK]
                for lag in range(LAGS)
            ]
            stacked = jnp.concatenate(parts, 0)
            first = pl.multiple_of(k * per_block, per_block)
            chunk = jnp.concatenate(
                [
                    jnp.concatenate([src_ref[first + j] for j in range(per_block)], 1)
                    for src_ref in src_refs
                ],
                0,
            )
            return acc + lax.dot_general(
                stacked, chunk, (((1,), (1,)), ((), ())), preferred_element_type=jnp.float32
            )

        acc = lax.fori_loop(
            0, samples // TIME_BLOCK, block, jnp.zeros((LAGS * chan_dev, rows), jnp.float32)
        )
        result = acc.T * factor_ref[0, 0]
        for j in range(blocks):
            out_ref[j] = result[:, j * out_width : (j + 1) * out_width]

    return pl.pallas_call(
        kernel,
        out_shape=jax.ShapeDtypeStruct((blocks, rows, out_width), jnp.float32),
        in_specs=[pl.BlockSpec(memory_space=pltpu.SMEM)]
        + [pl.BlockSpec(memory_space=pltpu.VMEM) for _ in range(len(halves) + 1)],
        out_specs=pl.BlockSpec(memory_space=pltpu.VMEM),
        scratch_shapes=[pltpu.VMEM((chan_dev, samples + 2 * EDGE), whitened.dtype)],
    )(factor.reshape(1, 1), *halves, whitened)


def body(traces, owner, window_mask):
    chan_dev = traces.shape[1]
    samples = traces.shape[2]
    step_count = owner.shape[0]
    chan_size = lax.axis_size("chan")
    win_size = lax.axis_size("win")
    chan_me = lax.axis_index("chan")
    win_me = lax.axis_index("win")
    signal = traces[0].astype(jnp.float32)
    whitened = (
        signal * lax.rsqrt(jnp.mean(signal * signal, axis=-1, keepdims=True) + 1e-06)
    ).astype(jnp.bfloat16)
    own_flag = window_mask[0, 0].astype(jnp.float32)
    outgoing = whitened * own_flag.astype(jnp.bfloat16)
    masked = jnp.concatenate(
        [jnp.where(chan_me == owner[step], outgoing, jnp.zeros_like(outgoing)) for step in range(step_count)],
        0,
    )
    rows = masked.shape[0]
    masked = masked.reshape(rows, chan_size, samples // chan_size).transpose(1, 0, 2)
    half = rows // 2
    halves = [
        broadcast(masked[:, which * half : (which + 1) * half], chan_me, "chan", chan_size, order)
        for which, order in enumerate(CHAN_BITS)
    ]
    factor = own_flag / math.sqrt(samples)
    complete = correlate(halves, whitened, factor, win_size)
    reduced = jnp.sum(lax.all_to_all(complete, "win", 0, 0, tiled=True), 0)
    per_dev = LAGS // win_size
    return reduced.reshape(step_count, chan_dev, per_dev, chan_dev)


def solution(mesh):
    return jax.shard_map(
        body,
        mesh=mesh,
        in_specs=(P("win", "chan", None), P(), P("win", "chan")),
        out_specs=P(None, None, "win", "chan"),
        check_vma=False,
    )
```

```python
import math

import jax
import jax.numpy as jnp
from jax import lax
from jax.experimental import pallas as pl
from jax.experimental.pallas import tpu as pltpu
from jax.sharding import PartitionSpec as P

LAGS = 64
EDGE = 128
TIME_BLOCK = 2048
CHAN_BITS = (((0,), (1,), (4,), (2, 3)), ((0,), (4,), (1,), (2, 3)))

def digit_of(me, bits):
    digit = 0
    for bit in bits:
        digit = digit * 2 + ((me >> bit) & 1)
    return digit


def flip_mask(bits, offset):
    mask = 0
    for place, bit in enumerate(bits):
        if (offset >> (len(bits) - 1 - place)) & 1:
            mask |= 1 << bit
    return mask


def xor_pairs(size, mask):
    return [(i, i ^ mask) for i in range(size)]


def broadcast(masked, me, axis, size, order):
    pieces = masked
    for bits in order:
        radix = 1 << len(bits)
        quarters = pieces.reshape(radix, pieces.shape[0] // radix, *pieces.shape[1:])
        digit = digit_of(me, bits)
        pieces = lax.dynamic_index_in_dim(quarters, digit, 0, keepdims=False)
        for offset in range(1, radix):
            send = lax.dynamic_index_in_dim(quarters, digit ^ offset, 0, keepdims=False)
            pieces = pieces + lax.ppermute(send, axis, xor_pairs(size, flip_mask(bits, offset)))
    for place, bits in enumerate(reversed(order)):
        radix = 1 << len(bits)
        digit = digit_of(me, bits)
        got = [pieces] + [
            lax.ppermute(pieces, axis, xor_pairs(size, flip_mask(bits, offset)))
            for offset in range(1, radix)
        ]
        if place == len(order) - 1 and radix == 2:
            return got[0], got[1], digit
        slots = []
        for slot in range(radix):
            offset = slot ^ digit
            value = got[0]
            for other in range(1, radix):
                value = jnp.where(offset == other, got[other], value)
            slots.append(value)
        pieces = jnp.concatenate(slots, 0)
    return pieces


def correlate(halves, digit, whitened, factor, blocks):
    piece_half, rows_half, piece_width = halves[0][0].shape
    rows = rows_half * len(halves)
    chan_dev, samples = whitened.shape
    per_block = TIME_BLOCK // piece_width
    width = TIME_BLOCK + 2 * EDGE
    out_width = LAGS * chan_dev // blocks
    count = 2 * len(halves)

    def kernel(factor_ref, digit_ref, *refs):
        src_refs, w_ref, out_ref, pad_ref = refs[:count], refs[count], refs[-2], refs[-1]
        low_is_mine = digit_ref[0, 0] == 0
        pad_ref[:, :EDGE] = jnp.zeros((chan_dev, EDGE), pad_ref.dtype)
        pad_ref[:, EDGE + samples :] = jnp.zeros((chan_dev, EDGE), pad_ref.dtype)
        pad_ref[:, EDGE : EDGE + samples] = w_ref[...]

        def piece(which, index):
            mine, other = src_refs[2 * which], src_refs[2 * which + 1]
            local = index % piece_half
            if index < piece_half:
                return jnp.where(low_is_mine, mine[local], other[local])
            return jnp.where(low_is_mine, other[local], mine[local])

        acc = jnp.zeros((LAGS * chan_dev, rows), jnp.float32)
        for k in range(samples // TIME_BLOCK):
            base = k * TIME_BLOCK
            window = pad_ref[:, base : base + width]
            parts = [
                pltpu.roll(window, width - (EDGE - LAGS // 2 + lag), 1)[:, :TIME_BLOCK]
                for lag in range(LAGS)
            ]
            stacked = jnp.concatenate(parts, 0)
            chunk = jnp.concatenate(
                [
                    jnp.concatenate([piece(which, k * per_block + j) for j in range(per_block)], 1)
                    for which in range(len(halves))
                ],
                0,
            )
            acc = acc + lax.dot_general(
                stacked, chunk, (((1,), (1,)), ((), ())), preferred_element_type=jnp.float32
            )
        result = acc.T * factor_ref[0, 0]
        for j in range(blocks):
            out_ref[j] = result[:, j * out_width : (j + 1) * out_width]

    return pl.pallas_call(
        kernel,
        out_shape=jax.ShapeDtypeStruct((blocks, rows, out_width), jnp.float32),
        in_specs=[pl.BlockSpec(memory_space=pltpu.SMEM), pl.BlockSpec(memory_space=pltpu.SMEM)]
        + [pl.BlockSpec(memory_space=pltpu.VMEM) for _ in range(count + 1)],
        out_specs=pl.BlockSpec(memory_space=pltpu.VMEM),
        scratch_shapes=[pltpu.VMEM((chan_dev, samples + 2 * EDGE), whitened.dtype)],
    )(
        factor.reshape(1, 1),
        digit.astype(jnp.int32).reshape(1, 1),
        *[part for half in halves for part in half],
        whitened,
    )


def body(traces, owner, window_mask):
    chan_dev = traces.shape[1]
    samples = traces.shape[2]
    step_count = owner.shape[0]
    chan_size = lax.axis_size("chan")
    win_size = lax.axis_size("win")
    chan_me = lax.axis_index("chan")
    win_me = lax.axis_index("win")
    signal = traces[0].astype(jnp.float32)
    whitened = (
        signal * lax.rsqrt(jnp.mean(signal * signal, axis=-1, keepdims=True) + 1e-06)
    ).astype(jnp.bfloat16)
    own_flag = window_mask[0, 0].astype(jnp.float32)
    outgoing = whitened * own_flag.astype(jnp.bfloat16)
    masked = jnp.concatenate(
        [jnp.where(chan_me == owner[step], outgoing, jnp.zeros_like(outgoing)) for step in range(step_count)],
        0,
    )
    rows = masked.shape[0]
    masked = masked.reshape(rows, chan_size, samples // chan_size).transpose(1, 0, 2)
    half = rows // 2
    whitened, masked = lax.optimization_barrier((whitened, masked))
    halves = []
    for which, order in enumerate(CHAN_BITS):
        mine, other, digit = broadcast(
            masked[:, which * half : (which + 1) * half], chan_me, "chan", chan_size, order
        )
        halves.append((mine, other))
    factor = own_flag / math.sqrt(samples)
    complete = correlate(halves, digit, whitened, factor, win_size)
    reduced = jnp.sum(lax.all_to_all(complete, "win", 0, 0, tiled=True), 0)
    per_dev = LAGS // win_size
    return reduced.reshape(step_count, chan_dev, per_dev, chan_dev)


def solution(mesh):
    return jax.shard_map(
        body,
        mesh=mesh,
        in_specs=(P("win", "chan", None), P(), P("win", "chan")),
        out_specs=P(None, None, "win", "chan"),
        check_vma=False,
    )
```

```python
import math

import jax
import jax.numpy as jnp
from jax import lax
from jax.experimental import pallas as pl
from jax.experimental.pallas import tpu as pltpu
from jax.sharding import PartitionSpec as P

LAGS = 64
EDGE = 128
TIME_BLOCK = 2048
CHAN_BITS = (((0,), (1,), (4,), (2, 3)), ((0,), (4,), (1,), (2, 3)))

def digit_of(me, bits):
    digit = 0
    for bit in bits:
        digit = digit * 2 + ((me >> bit) & 1)
    return digit


def flip_mask(bits, offset):
    mask = 0
    for place, bit in enumerate(bits):
        if (offset >> (len(bits) - 1 - place)) & 1:
            mask |= 1 << bit
    return mask


def xor_pairs(size, mask):
    return [(i, i ^ mask) for i in range(size)]


def broadcast(masked, me, axis, size, order, rider):
    pieces = masked
    for place, bits in enumerate(order):
        radix = 1 << len(bits)
        quarters = pieces.reshape(radix, pieces.shape[0] // radix, *pieces.shape[1:])
        digit = digit_of(me, bits)
        pieces = lax.dynamic_index_in_dim(quarters, digit, 0, keepdims=False)
        for offset in range(1, radix):
            send = lax.dynamic_index_in_dim(quarters, digit ^ offset, 0, keepdims=False)
            pieces = pieces + lax.ppermute(send, axis, xor_pairs(size, flip_mask(bits, offset)))
        if place == 0:
            pieces, rider = lax.optimization_barrier((pieces, rider))
    for place, bits in enumerate(reversed(order)):
        radix = 1 << len(bits)
        digit = digit_of(me, bits)
        got = [pieces] + [
            lax.ppermute(pieces, axis, xor_pairs(size, flip_mask(bits, offset)))
            for offset in range(1, radix)
        ]
        if place == len(order) - 1 and radix == 2:
            return got[0], got[1], digit, rider
        slots = []
        for slot in range(radix):
            offset = slot ^ digit
            value = got[0]
            for other in range(1, radix):
                value = jnp.where(offset == other, got[other], value)
            slots.append(value)
        pieces = jnp.concatenate(slots, 0)
    return pieces


def correlate(halves, digit, whitened, factor, blocks):
    piece_half, rows_half, piece_width = halves[0][0].shape
    rows = rows_half * len(halves)
    chan_dev, samples = whitened.shape
    per_block = TIME_BLOCK // piece_width
    width = TIME_BLOCK + 2 * EDGE
    out_width = LAGS * chan_dev // blocks
    count = 2 * len(halves)

    def kernel(factor_ref, digit_ref, *refs):
        src_refs, w_ref, out_ref, pad_ref = refs[:count], refs[count], refs[-2], refs[-1]
        low_is_mine = digit_ref[0, 0] == 0
        pad_ref[:, :EDGE] = jnp.zeros((chan_dev, EDGE), pad_ref.dtype)
        pad_ref[:, EDGE + samples :] = jnp.zeros((chan_dev, EDGE), pad_ref.dtype)
        pad_ref[:, EDGE : EDGE + samples] = w_ref[...]

        def piece(which, index):
            mine, other = src_refs[2 * which], src_refs[2 * which + 1]
            local = index % piece_half
            if index < piece_half:
                return jnp.where(low_is_mine, mine[local], other[local])
            return jnp.where(low_is_mine, other[local], mine[local])

        acc = jnp.zeros((LAGS * chan_dev, rows), jnp.float32)
        for k in range(samples // TIME_BLOCK):
            base = k * TIME_BLOCK
            window = pad_ref[:, base : base + width]
            parts = [
                pltpu.roll(window, width - (EDGE - LAGS // 2 + lag), 1)[:, :TIME_BLOCK]
                for lag in range(LAGS)
            ]
            stacked = jnp.concatenate(parts, 0)
            chunk = jnp.concatenate(
                [
                    jnp.concatenate([piece(which, k * per_block + j) for j in range(per_block)], 1)
                    for which in range(len(halves))
                ],
                0,
            )
            acc = acc + lax.dot_general(
                stacked, chunk, (((1,), (1,)), ((), ())), preferred_element_type=jnp.float32
            )
        result = acc.T * factor_ref[0, 0]
        for j in range(blocks):
            out_ref[j] = result[:, j * out_width : (j + 1) * out_width]

    return pl.pallas_call(
        kernel,
        out_shape=jax.ShapeDtypeStruct((blocks, rows, out_width), jnp.float32),
        in_specs=[pl.BlockSpec(memory_space=pltpu.SMEM), pl.BlockSpec(memory_space=pltpu.SMEM)]
        + [pl.BlockSpec(memory_space=pltpu.VMEM) for _ in range(count + 1)],
        out_specs=pl.BlockSpec(memory_space=pltpu.VMEM),
        scratch_shapes=[pltpu.VMEM((chan_dev, samples + 2 * EDGE), whitened.dtype)],
    )(
        factor.reshape(1, 1),
        digit.astype(jnp.int32).reshape(1, 1),
        *[part for half in halves for part in half],
        whitened,
    )


def body(traces, owner, window_mask):
    chan_dev = traces.shape[1]
    samples = traces.shape[2]
    step_count = owner.shape[0]
    chan_size = lax.axis_size("chan")
    win_size = lax.axis_size("win")
    chan_me = lax.axis_index("chan")
    win_me = lax.axis_index("win")
    signal = traces[0].astype(jnp.float32)
    scale = lax.rsqrt(jnp.mean(signal * signal, axis=-1, keepdims=True) + 1e-06)
    whitened = (signal * scale).astype(jnp.bfloat16)
    own_flag = window_mask[0, 0].astype(jnp.float32)
    pieces = traces[0].reshape(chan_dev, chan_size, samples // chan_size).transpose(1, 0, 2)
    outgoing = (pieces.astype(jnp.float32) * scale[None]).astype(jnp.bfloat16) * own_flag.astype(
        jnp.bfloat16
    )
    masked = jnp.concatenate(
        [jnp.where(chan_me == owner[step], outgoing, jnp.zeros_like(outgoing)) for step in range(step_count)],
        1,
    )
    half = masked.shape[1] // 2
    halves = []
    rider = whitened
    for which, order in enumerate(CHAN_BITS):
        mine, other, digit, rider = broadcast(
            masked[:, which * half : (which + 1) * half], chan_me, "chan", chan_size, order, rider
        )
        halves.append((mine, other))
    whitened = rider
    factor = own_flag / math.sqrt(samples)
    complete = correlate(halves, digit, whitened, factor, win_size)
    reduced = jnp.sum(lax.all_to_all(complete, "win", 0, 0, tiled=True), 0)
    per_dev = LAGS // win_size
    return reduced.reshape(step_count, chan_dev, per_dev, chan_dev)


def solution(mesh):
    return jax.shard_map(
        body,
        mesh=mesh,
        in_specs=(P("win", "chan", None), P(), P("win", "chan")),
        out_specs=P(None, None, "win", "chan"),
        check_vma=False,
    )
```

```python
import math

import jax
import jax.numpy as jnp
from jax import lax
from jax.experimental import pallas as pl
from jax.experimental.pallas import tpu as pltpu
from jax.sharding import PartitionSpec as P

LAGS = 64
EDGE = 128
TIME_BLOCK = 2048
CHAN_BITS = (((0,), (1, 4), (2, 3)), ((0,), (1, 4), (2, 3)))

def digit_of(me, bits):
    digit = 0
    for bit in bits:
        digit = digit * 2 + ((me >> bit) & 1)
    return digit


def flip_mask(bits, offset):
    mask = 0
    for place, bit in enumerate(bits):
        if (offset >> (len(bits) - 1 - place)) & 1:
            mask |= 1 << bit
    return mask


def xor_pairs(size, mask):
    return [(i, i ^ mask) for i in range(size)]


def broadcast(masked, me, axis, size, order, rider):
    pieces = masked
    for place, bits in enumerate(order):
        radix = 1 << len(bits)
        quarters = pieces.reshape(radix, pieces.shape[0] // radix, *pieces.shape[1:])
        digit = digit_of(me, bits)
        pieces = lax.dynamic_index_in_dim(quarters, digit, 0, keepdims=False)
        for offset in range(1, radix):
            send = lax.dynamic_index_in_dim(quarters, digit ^ offset, 0, keepdims=False)
            pieces = pieces + lax.ppermute(send, axis, xor_pairs(size, flip_mask(bits, offset)))
        if place == 0:
            pieces, rider = lax.optimization_barrier((pieces, rider))
    for place, bits in enumerate(reversed(order)):
        radix = 1 << len(bits)
        digit = digit_of(me, bits)
        got = [pieces] + [
            lax.ppermute(pieces, axis, xor_pairs(size, flip_mask(bits, offset)))
            for offset in range(1, radix)
        ]
        if place == len(order) - 1 and radix == 2:
            return got[0], got[1], digit, rider
        slots = []
        for slot in range(radix):
            offset = slot ^ digit
            value = got[0]
            for other in range(1, radix):
                value = jnp.where(offset == other, got[other], value)
            slots.append(value)
        pieces = jnp.concatenate(slots, 0)
    return pieces


def correlate(halves, digit, whitened, factor, blocks):
    piece_half, rows_half, piece_width = halves[0][0].shape
    rows = rows_half * len(halves)
    chan_dev, samples = whitened.shape
    per_block = TIME_BLOCK // piece_width
    width = TIME_BLOCK + 2 * EDGE
    out_width = LAGS * chan_dev // blocks
    count = 2 * len(halves)

    def kernel(factor_ref, digit_ref, *refs):
        src_refs, w_ref, out_ref, pad_ref = refs[:count], refs[count], refs[-2], refs[-1]
        low_is_mine = digit_ref[0, 0] == 0
        pad_ref[:, :EDGE] = jnp.zeros((chan_dev, EDGE), pad_ref.dtype)
        pad_ref[:, EDGE + samples :] = jnp.zeros((chan_dev, EDGE), pad_ref.dtype)
        pad_ref[:, EDGE : EDGE + samples] = w_ref[...]

        def piece(which, index):
            mine, other = src_refs[2 * which], src_refs[2 * which + 1]
            local = index % piece_half
            if index < piece_half:
                return jnp.where(low_is_mine, mine[local], other[local])
            return jnp.where(low_is_mine, other[local], mine[local])

        acc = jnp.zeros((LAGS * chan_dev, rows), jnp.float32)
        for k in range(samples // TIME_BLOCK):
            base = k * TIME_BLOCK
            window = pad_ref[:, base : base + width]
            parts = [
                pltpu.roll(window, width - (EDGE - LAGS // 2 + lag), 1)[:, :TIME_BLOCK]
                for lag in range(LAGS)
            ]
            stacked = jnp.concatenate(parts, 0)
            chunk = jnp.concatenate(
                [
                    jnp.concatenate([piece(which, k * per_block + j) for j in range(per_block)], 1)
                    for which in range(len(halves))
                ],
                0,
            )
            acc = acc + lax.dot_general(
                stacked, chunk, (((1,), (1,)), ((), ())), preferred_element_type=jnp.float32
            )
        result = acc.T * factor_ref[0, 0]
        for j in range(blocks):
            out_ref[j] = result[:, j * out_width : (j + 1) * out_width]

    return pl.pallas_call(
        kernel,
        out_shape=jax.ShapeDtypeStruct((blocks, rows, out_width), jnp.float32),
        in_specs=[pl.BlockSpec(memory_space=pltpu.SMEM), pl.BlockSpec(memory_space=pltpu.SMEM)]
        + [pl.BlockSpec(memory_space=pltpu.VMEM) for _ in range(count + 1)],
        out_specs=pl.BlockSpec(memory_space=pltpu.VMEM),
        scratch_shapes=[pltpu.VMEM((chan_dev, samples + 2 * EDGE), whitened.dtype)],
    )(
        factor.reshape(1, 1),
        digit.astype(jnp.int32).reshape(1, 1),
        *[part for half in halves for part in half],
        whitened,
    )


def body(traces, owner, window_mask):
    chan_dev = traces.shape[1]
    samples = traces.shape[2]
    step_count = owner.shape[0]
    chan_size = lax.axis_size("chan")
    win_size = lax.axis_size("win")
    chan_me = lax.axis_index("chan")
    win_me = lax.axis_index("win")
    signal = traces[0].astype(jnp.float32)
    scale = lax.rsqrt(jnp.mean(signal * signal, axis=-1, keepdims=True) + 1e-06)
    whitened = (signal * scale).astype(jnp.bfloat16)
    own_flag = window_mask[0, 0].astype(jnp.float32)
    pieces = traces[0].reshape(chan_dev, chan_size, samples // chan_size).transpose(1, 0, 2)
    outgoing = (pieces.astype(jnp.float32) * scale[None]).astype(jnp.bfloat16) * own_flag.astype(
        jnp.bfloat16
    )
    masked = jnp.concatenate(
        [jnp.where(chan_me == owner[step], outgoing, jnp.zeros_like(outgoing)) for step in range(step_count)],
        1,
    )
    half = masked.shape[1] // 2
    halves = []
    rider = whitened
    for which, order in enumerate(CHAN_BITS):
        mine, other, digit, rider = broadcast(
            masked[:, which * half : (which + 1) * half], chan_me, "chan", chan_size, order, rider
        )
        halves.append((mine, other))
    whitened = rider
    factor = own_flag / math.sqrt(samples)
    complete = correlate(halves, digit, whitened, factor, win_size)
    reduced = jnp.sum(lax.all_to_all(complete, "win", 0, 0, tiled=True), 0)
    per_dev = LAGS // win_size
    return reduced.reshape(step_count, chan_dev, per_dev, chan_dev)


def solution(mesh):
    return jax.shard_map(
        body,
        mesh=mesh,
        in_specs=(P("win", "chan", None), P(), P("win", "chan")),
        out_specs=P(None, None, "win", "chan"),
        check_vma=False,
    )
```

```python
import math

import jax
import jax.numpy as jnp
from jax import lax
from jax.experimental import pallas as pl
from jax.experimental.pallas import tpu as pltpu
from jax.sharding import PartitionSpec as P

LAGS = 64
EDGE = 128
TIME_BLOCK = 4096
CHAN_BITS = (((0,), (1, 4), (2, 3)), ((0,), (1, 4), (2, 3)))

def digit_of(me, bits):
    digit = 0
    for bit in bits:
        digit = digit * 2 + ((me >> bit) & 1)
    return digit


def flip_mask(bits, offset):
    mask = 0
    for place, bit in enumerate(bits):
        if (offset >> (len(bits) - 1 - place)) & 1:
            mask |= 1 << bit
    return mask


def xor_pairs(size, mask):
    return [(i, i ^ mask) for i in range(size)]


def broadcast(masked, me, axis, size, order, rider):
    pieces = masked
    for place, bits in enumerate(order):
        radix = 1 << len(bits)
        quarters = pieces.reshape(radix, pieces.shape[0] // radix, *pieces.shape[1:])
        digit = digit_of(me, bits)
        pieces = lax.dynamic_index_in_dim(quarters, digit, 0, keepdims=False)
        for offset in range(1, radix):
            send = lax.dynamic_index_in_dim(quarters, digit ^ offset, 0, keepdims=False)
            pieces = pieces + lax.ppermute(send, axis, xor_pairs(size, flip_mask(bits, offset)))
        if place == 0:
            pieces, rider = lax.optimization_barrier((pieces, rider))
    for place, bits in enumerate(reversed(order)):
        radix = 1 << len(bits)
        digit = digit_of(me, bits)
        got = [pieces] + [
            lax.ppermute(pieces, axis, xor_pairs(size, flip_mask(bits, offset)))
            for offset in range(1, radix)
        ]
        if place == len(order) - 1 and radix == 2:
            return got[0], got[1], digit, rider
        slots = []
        for slot in range(radix):
            offset = slot ^ digit
            value = got[0]
            for other in range(1, radix):
                value = jnp.where(offset == other, got[other], value)
            slots.append(value)
        pieces = jnp.concatenate(slots, 0)
    return pieces


def correlate(halves, digit, whitened, factor, blocks):
    piece_half, rows_half, piece_width = halves[0][0].shape
    rows = rows_half * len(halves)
    chan_dev, samples = whitened.shape
    per_block = TIME_BLOCK // piece_width
    width = TIME_BLOCK + 2 * EDGE
    out_width = LAGS * chan_dev // blocks
    count = 2 * len(halves)

    def kernel(factor_ref, digit_ref, *refs):
        src_refs, w_ref, out_ref, pad_ref = refs[:count], refs[count], refs[-2], refs[-1]
        low_is_mine = digit_ref[0, 0] == 0
        pad_ref[:, :EDGE] = jnp.zeros((chan_dev, EDGE), pad_ref.dtype)
        pad_ref[:, EDGE + samples :] = jnp.zeros((chan_dev, EDGE), pad_ref.dtype)
        pad_ref[:, EDGE : EDGE + samples] = w_ref[...]

        def piece(which, index):
            mine, other = src_refs[2 * which], src_refs[2 * which + 1]
            local = index % piece_half
            if index < piece_half:
                return jnp.where(low_is_mine, mine[local], other[local])
            return jnp.where(low_is_mine, other[local], mine[local])

        acc = jnp.zeros((LAGS * chan_dev, rows), jnp.float32)
        for k in range(samples // TIME_BLOCK):
            base = k * TIME_BLOCK
            window = pad_ref[:, base : base + width]
            parts = [
                pltpu.roll(window, width - (EDGE - LAGS // 2 + lag), 1)[:, :TIME_BLOCK]
                for lag in range(LAGS)
            ]
            stacked = jnp.concatenate(parts, 0)
            chunk = jnp.concatenate(
                [
                    jnp.concatenate([piece(which, k * per_block + j) for j in range(per_block)], 1)
                    for which in range(len(halves))
                ],
                0,
            )
            acc = acc + lax.dot_general(
                stacked, chunk, (((1,), (1,)), ((), ())), preferred_element_type=jnp.float32
            )
        result = acc.T * factor_ref[0, 0]
        for j in range(blocks):
            out_ref[j] = result[:, j * out_width : (j + 1) * out_width]

    return pl.pallas_call(
        kernel,
        out_shape=jax.ShapeDtypeStruct((blocks, rows, out_width), jnp.float32),
        in_specs=[pl.BlockSpec(memory_space=pltpu.SMEM), pl.BlockSpec(memory_space=pltpu.SMEM)]
        + [pl.BlockSpec(memory_space=pltpu.VMEM) for _ in range(count + 1)],
        out_specs=pl.BlockSpec(memory_space=pltpu.VMEM),
        scratch_shapes=[pltpu.VMEM((chan_dev, samples + 2 * EDGE), whitened.dtype)],
    )(
        factor.reshape(1, 1),
        digit.astype(jnp.int32).reshape(1, 1),
        *[part for half in halves for part in half],
        whitened,
    )


def body(traces, owner, window_mask):
    chan_dev = traces.shape[1]
    samples = traces.shape[2]
    step_count = owner.shape[0]
    chan_size = lax.axis_size("chan")
    win_size = lax.axis_size("win")
    chan_me = lax.axis_index("chan")
    win_me = lax.axis_index("win")
    signal = traces[0].astype(jnp.float32)
    scale = lax.rsqrt(jnp.mean(signal * signal, axis=-1, keepdims=True) + 1e-06)
    whitened = (signal * scale).astype(jnp.bfloat16)
    own_flag = window_mask[0, 0].astype(jnp.float32)
    pieces = traces[0].reshape(chan_dev, chan_size, samples // chan_size).transpose(1, 0, 2)
    outgoing = (pieces.astype(jnp.float32) * scale[None]).astype(jnp.bfloat16) * own_flag.astype(
        jnp.bfloat16
    )
    masked = jnp.concatenate(
        [jnp.where(chan_me == owner[step], outgoing, jnp.zeros_like(outgoing)) for step in range(step_count)],
        1,
    )
    half = masked.shape[1] // 2
    halves = []
    rider = whitened
    for which, order in enumerate(CHAN_BITS):
        mine, other, digit, rider = broadcast(
            masked[:, which * half : (which + 1) * half], chan_me, "chan", chan_size, order, rider
        )
        halves.append((mine, other))
    whitened = rider
    factor = own_flag / math.sqrt(samples)
    complete = correlate(halves, digit, whitened, factor, win_size)
    reduced = jnp.sum(lax.all_to_all(complete, "win", 0, 0, tiled=True), 0)
    per_dev = LAGS // win_size
    return reduced.reshape(step_count, chan_dev, per_dev, chan_dev)


def solution(mesh):
    return jax.shard_map(
        body,
        mesh=mesh,
        in_specs=(P("win", "chan", None), P(), P("win", "chan")),
        out_specs=P(None, None, "win", "chan"),
        check_vma=False,
    )
```

```python
import math

import jax
import jax.numpy as jnp
from jax import lax
from jax.experimental import pallas as pl
from jax.experimental.pallas import tpu as pltpu
from jax.sharding import PartitionSpec as P

LAGS = 64
EDGE = 128
TIME_BLOCK = 4096
CHAN_BITS = (((0,), (1, 4), (2, 3)), ((0,), (1, 4), (2, 3)))

def digit_of(me, bits):
    digit = 0
    for bit in bits:
        digit = digit * 2 + ((me >> bit) & 1)
    return digit


def flip_mask(bits, offset):
    mask = 0
    for place, bit in enumerate(bits):
        if (offset >> (len(bits) - 1 - place)) & 1:
            mask |= 1 << bit
    return mask


def xor_pairs(size, mask):
    return [(i, i ^ mask) for i in range(size)]


def broadcast(masked, me, axis, size, order, rider):
    pieces = masked
    for place, bits in enumerate(order):
        radix = 1 << len(bits)
        quarters = pieces.reshape(radix, pieces.shape[0] // radix, *pieces.shape[1:])
        digit = digit_of(me, bits)
        pieces = lax.dynamic_index_in_dim(quarters, digit, 0, keepdims=False)
        for offset in range(1, radix):
            send = lax.dynamic_index_in_dim(quarters, digit ^ offset, 0, keepdims=False)
            pieces = pieces + lax.ppermute(send, axis, xor_pairs(size, flip_mask(bits, offset)))
        if place == 0:
            pieces, rider = lax.optimization_barrier((pieces, rider))
    for place, bits in enumerate(reversed(order)):
        radix = 1 << len(bits)
        digit = digit_of(me, bits)
        got = [pieces] + [
            lax.ppermute(pieces, axis, xor_pairs(size, flip_mask(bits, offset)))
            for offset in range(1, radix)
        ]
        if place == len(order) - 1 and radix == 2:
            return got[0], got[1], digit, rider
        slots = []
        for slot in range(radix):
            offset = slot ^ digit
            value = got[0]
            for other in range(1, radix):
                value = jnp.where(offset == other, got[other], value)
            slots.append(value)
        pieces = jnp.concatenate(slots, 0)
    return pieces


def correlate(halves, digit, whitened, factor, blocks):
    piece_half, rows_half, piece_width = halves[0][0].shape
    rows = rows_half * len(halves)
    chan_dev, samples = whitened.shape
    per_block = TIME_BLOCK // piece_width
    width = TIME_BLOCK + 2 * EDGE
    out_width = LAGS * chan_dev // blocks
    count = 2 * len(halves)

    def kernel(factor_ref, digit_ref, *refs):
        src_refs, w_ref, out_ref, pad_ref = refs[:count], refs[count], refs[-2], refs[-1]
        low_is_mine = digit_ref[0, 0] == 0
        pad_ref[:, :EDGE] = jnp.zeros((chan_dev, EDGE), pad_ref.dtype)
        pad_ref[:, EDGE + samples :] = jnp.zeros((chan_dev, EDGE), pad_ref.dtype)
        pad_ref[:, EDGE : EDGE + samples] = w_ref[...]

        def piece(which, index):
            mine, other = src_refs[2 * which], src_refs[2 * which + 1]
            local = index % piece_half
            if index < piece_half:
                return jnp.where(low_is_mine, mine[local], other[local])
            return jnp.where(low_is_mine, other[local], mine[local])

        acc = jnp.zeros((LAGS * chan_dev, rows), jnp.float32)
        for k in range(samples // TIME_BLOCK):
            base = k * TIME_BLOCK
            window = pad_ref[:, base : base + width]
            parts = [
                pltpu.roll(window, width - (EDGE - LAGS // 2 + lag), 1)[:, :TIME_BLOCK]
                for lag in range(LAGS)
            ]
            stacked = jnp.concatenate(parts, 0)
            chunk = jnp.concatenate(
                [
                    jnp.concatenate([piece(which, k * per_block + j) for j in range(per_block)], 1)
                    for which in range(len(halves))
                ],
                0,
            )
            acc = acc + lax.dot_general(
                stacked, chunk, (((1,), (1,)), ((), ())), preferred_element_type=jnp.float32
            )
        result = acc.T * factor_ref[0, 0]
        for j in range(blocks):
            out_ref[j] = result[:, j * out_width : (j + 1) * out_width]

    return pl.pallas_call(
        kernel,
        out_shape=jax.ShapeDtypeStruct((blocks, rows, out_width), jnp.float32),
        in_specs=[pl.BlockSpec(memory_space=pltpu.SMEM), pl.BlockSpec(memory_space=pltpu.SMEM)]
        + [pl.BlockSpec(memory_space=pltpu.VMEM) for _ in range(count + 1)],
        out_specs=pl.BlockSpec(memory_space=pltpu.VMEM),
        scratch_shapes=[pltpu.VMEM((chan_dev, samples + 2 * EDGE), whitened.dtype)],
    )(
        factor.reshape(1, 1),
        digit.astype(jnp.int32).reshape(1, 1),
        *[part for half in halves for part in half],
        whitened,
    )


def body(traces, owner, window_mask):
    chan_dev = traces.shape[1]
    samples = traces.shape[2]
    step_count = owner.shape[0]
    chan_size = lax.axis_size("chan")
    win_size = lax.axis_size("win")
    chan_me = lax.axis_index("chan")
    win_me = lax.axis_index("win")
    signal = traces[0].astype(jnp.float32)
    scale = lax.rsqrt(jnp.mean(signal * signal, axis=-1, keepdims=True) + 1e-06)
    whitened = (signal * scale).astype(jnp.bfloat16)
    own_flag = window_mask[0, 0].astype(jnp.float32)
    pieces = traces[0].reshape(chan_dev, chan_size, samples // chan_size).transpose(1, 0, 2)
    outgoing = (pieces.astype(jnp.float32) * scale[None]).astype(jnp.bfloat16) * own_flag.astype(
        jnp.bfloat16
    )
    hits = (owner == chan_me)[None, :, None, None]
    masked = jnp.where(hits, outgoing[:, None], jnp.zeros_like(outgoing)[:, None])
    masked = masked.reshape(chan_size, step_count * chan_dev, samples // chan_size)
    half = masked.shape[1] // 2
    halves = []
    rider = whitened
    for which, order in enumerate(CHAN_BITS):
        mine, other, digit, rider = broadcast(
            masked[:, which * half : (which + 1) * half], chan_me, "chan", chan_size, order, rider
        )
        halves.append((mine, other))
    whitened = rider
    factor = own_flag / math.sqrt(samples)
    complete = correlate(halves, digit, whitened, factor, win_size)
    reduced = jnp.sum(lax.all_to_all(complete, "win", 0, 0, tiled=True), 0)
    per_dev = LAGS // win_size
    return reduced.reshape(step_count, chan_dev, per_dev, chan_dev)


def solution(mesh):
    return jax.shard_map(
        body,
        mesh=mesh,
        in_specs=(P("win", "chan", None), P(), P("win", "chan")),
        out_specs=P(None, None, "win", "chan"),
        check_vma=False,
    )
```
